512 devices in a mesh: template: 16 (over y, x_hi, core), fsdp: 16 (over z), dp: 2 (over x_lo).
Axes of the slice: x: 4 (x_hi: 2, x_lo: 2; x = x_hi * 2 + x_lo), y: 4, z: 16, core: 2. Of those that a mesh axis runs over, the one named last changes fastest.
Arguments:
- hidden: bfloat16 [16, 4096, 8192], P('template', ('fsdp', 'dp')), may hold values from -6 to 6
- target: bfloat16 [16, 4096, 512], P('template', ('fsdp', 'dp')), may hold values from -6 to 6
- weight: bfloat16 [16, 8192, 512], P('template', 'fsdp'), may hold values from -6 to 6
- gain: bfloat16 [16, 8192], P('template', 'fsdp'), may hold values from 0.099609375 to 1.8984375
Outputs:
- merged_weight: float32 [8192, 512], P(('fsdp', 'dp'))
- merged_gain: float32 [8192], P(('fsdp', 'dp'))
The draws below stay inside these ranges and needn't reach their ends.
All inputs are finite; a program needn't handle non-finite values.
Results may differ from the reference program's by a relative error of at most 0.0018.
Values may be sent and summed in bfloat16 or wider, within the bound.
No kernel may reach another device: no remote copies, remote signals or barrier semaphores. Data moves between devices by JAX's collectives and lax.ppermute only.
A program may use at most 64 MiB of HBM per device.

```python
import math
import jax
import jax.numpy as jnp
from jax import lax

D = 8192
HD = 512
TEMPLATES = 16
TOKENS = 4096


def spiked(array, own_key, source, target, blocks, factor):
    owner, partner = [(jnp.arange(array.shape[axis_at]) // (array.shape[axis_at] // blocks)).reshape([-1 if axis == axis_at else 1 for axis in range(array.ndim)]) for axis_at in (source, target)]
    chosen = jax.random.permutation(own_key, blocks)[partner]
    strong = (owner == chosen) | (owner == (partner + blocks // 2) % blocks)
    return jnp.where(strong, factor * array, array)


def levels(key, dims, split, smallest, high):
    level = 1.0
    for position, blocks in split:
        draws = jax.random.uniform(jax.random.fold_in(jax.random.fold_in(key, 6), position), (blocks,), jnp.float32, smallest / len(split), high / len(split))
        level = level * jnp.repeat(jnp.exp(draws), dims[position] // blocks).reshape((-1,) + (1,) * (len(dims) - 1 - position))
    return level


def gaussian(own_key, extent, deviation, reach, cuts=(), kind=jnp.bfloat16):
    entries = deviation * jax.random.normal(own_key, extent, jnp.float32)
    if cuts:
        entries = entries * levels(own_key, extent, cuts, -0.22, 0.18)
    return jnp.clip(entries, -reach, reach).astype(kind)


def bell_draw_with(rng, shape, width, reach, cuts, heavy, kind=jnp.bfloat16):
    result = width * jax.random.normal(rng, shape, jnp.float32)
    if cuts:
        result = result * levels(rng, shape, cuts, -0.22, 0.18)
    return jnp.clip(spiked(result, jax.random.fold_in(rng, 3), *heavy), -reach, reach).astype(kind)


def setup_inputs(seed: int = 0) -> dict:
    key_list = jax.random.split(jax.random.key(seed), 5)
    hidden = bell_draw_with(key_list[0], (TEMPLATES, TOKENS, D), 1.0, 6.0, ((0, 16), (1, 32)), (1, 2, 32, 2.75))
    target = gaussian(key_list[1], (TEMPLATES, TOKENS, HD), 1.0, 6.0, ((0, 16), (1, 32)))
    weight = gaussian(key_list[2], (TEMPLATES, D, HD), 1.0, 6.0, ((0, 16), (1, 16)))
    gain = jnp.clip(1.0 + 0.18 * jax.random.normal(key_list[3], (TEMPLATES, D), jnp.float32), 0.099609375, 1.8984375).astype(jnp.bfloat16)
    return dict(hidden=hidden, target=target, weight=weight, gain=gain)


def reference(hidden, target, weight, gain):
    scale = 1.0 / math.sqrt(D)

    def one_model(carry, index):
        num, den, gnum, gden = carry
        hidden_state = hidden[index].astype(jnp.float32)
        merge_quotient = lax.rsqrt(lax.optimization_barrier(jnp.mean(hidden_state * hidden_state, axis=1, keepdims=True)) + 1e-05)
        normalized_activation = hidden_state * merge_quotient
        gain_vector = gain[index].astype(jnp.float32)
        normalized_input = (normalized_activation * gain_vector[None, :]).astype(jnp.bfloat16)
        w = weight[index]
        values = jnp.dot(normalized_input, w, preferred_element_type=jnp.float32) * scale
        delta = (values - target[index].astype(jnp.float32)).astype(jnp.bfloat16)
        sq_normed = jnp.square(normalized_input.astype(jnp.float32)).astype(jnp.bfloat16)
        sq_delta = jnp.square(delta.astype(jnp.float32)).astype(jnp.bfloat16)
        fisher = jnp.dot(sq_normed.T, sq_delta, preferred_element_type=jnp.float32)
        backward_pass = jnp.dot(delta, w.T, preferred_element_type=jnp.float32) * scale
        gain_information_sum = lax.optimization_barrier(jnp.sum(jnp.square(backward_pass * normalized_activation), axis=0))
        wf = w.astype(jnp.float32)
        return ((num + fisher * wf, den + fisher, gnum + gain_information_sum * gain_vector, gden + gain_information_sum), None)
    start = (jnp.zeros((D, HD), jnp.float32), jnp.zeros((D, HD), jnp.float32), jnp.zeros((D,), jnp.float32), jnp.zeros((D,), jnp.float32))
    totals, unused = lax.scan(one_model, start, jnp.arange(TEMPLATES, dtype=jnp.int32))
    num, den, gnum, gden = totals
    return (num / den, gnum / gden)
```

```python
import math

import jax
import jax.numpy as jnp
from jax import lax
from jax.sharding import PartitionSpec as P


def body(hidden, target, weight, gain):
    token_batch = hidden[0]
    goal = target[0]
    w_shard = weight[0]
    g_shard = gain[0]
    width = token_batch.shape[1]
    rows = w_shard.shape[0]
    heads = w_shard.shape[1]
    scale = 1.0 / math.sqrt(width)
    n_t = lax.axis_size("template")
    n_dp = lax.axis_size("dp")

    hidden_f = token_batch.astype(jnp.float32)
    ratio = lax.rsqrt(jnp.mean(jnp.square(hidden_f), axis=1, keepdims=True) + 1e-05)
    w_full = lax.all_gather(w_shard, "fsdp", axis=0, tiled=True)
    g_full = lax.all_gather(g_shard, "fsdp", axis=0, tiled=True)
    xhat = hidden_f * ratio
    normed = (xhat * g_full.astype(jnp.float32)[None, :]).astype(jnp.bfloat16)
    values = jnp.dot(normed, w_full, preferred_element_type=jnp.float32) * scale
    delta = (values - goal.astype(jnp.float32)).astype(jnp.bfloat16)

    local_hidden = lax.all_to_all(token_batch, "fsdp", 1, 0, tiled=True)
    local_ratio = lax.all_gather(ratio, "fsdp", axis=0, tiled=True)
    local_delta = lax.all_gather(delta, "fsdp", axis=0, tiled=True)
    local_xhat = local_hidden.astype(jnp.float32) * local_ratio
    g_f = g_shard.astype(jnp.float32)
    local_normed = (local_xhat * g_f[None, :]).astype(jnp.bfloat16)
    sq_normed = jnp.square(local_normed.astype(jnp.float32)).astype(jnp.bfloat16)
    sq_delta = jnp.square(local_delta.astype(jnp.float32)).astype(jnp.bfloat16)
    fisher = jnp.einsum("td,th->dh", sq_normed, sq_delta, preferred_element_type=jnp.float32)
    back = jnp.einsum("th,dh->td", local_delta, w_shard, preferred_element_type=jnp.float32) * scale
    gain_info = jnp.sum(jnp.square(back * local_xhat), axis=0)

    extra = jnp.zeros((rows, 128), jnp.float32)
    extra = extra.at[:, 0].set(gain_info * g_f).at[:, 1].set(gain_info)
    pack = jnp.concatenate([fisher * w_shard.astype(jnp.float32), fisher, extra], axis=1)
    cols = pack.shape[1]
    piece = rows // (n_t * n_dp)
    pack = pack.reshape(n_dp, n_t, piece, cols).transpose(1, 0, 2, 3).reshape(n_t * n_dp, piece, cols)
    parts = lax.all_to_all(pack, ("template", "dp"), 0, 0, tiled=True)
    total = jnp.sum(parts, axis=0, keepdims=True)
    spread = lax.all_to_all(jnp.broadcast_to(total, (n_t, piece, cols)), "template", 0, 0, tiled=True)
    full = spread.reshape(n_t * piece, cols)
    merged = full[:, :heads] / full[:, heads : 2 * heads]
    merged_gain = full[:, 2 * heads] / full[:, 2 * heads + 1]
    return merged, merged_gain


def solution(mesh):
    in_specs = (
        P("template", ("fsdp", "dp"), None),
        P("template", ("fsdp", "dp"), None),
        P("template", "fsdp", None),
        P("template", "fsdp"),
    )
    out_specs = (P(("fsdp", "dp"), None), P(("fsdp", "dp")))
    return jax.shard_map(body, mesh=mesh, in_specs=in_specs, out_specs=out_specs, check_vma=False)
```

```python
import math

import jax
import jax.numpy as jnp
from jax import lax
from jax.sharding import PartitionSpec as P


def body(hidden, target, weight, gain):
    token_batch = hidden[0]
    goal = target[0]
    w_shard = weight[0]
    g_shard = gain[0]
    width = token_batch.shape[1]
    rows = w_shard.shape[0]
    heads = w_shard.shape[1]
    scale = 1.0 / math.sqrt(width)
    n_t = lax.axis_size("template")
    n_dp = lax.axis_size("dp")

    hidden_f = token_batch.astype(jnp.float32)
    ratio = lax.rsqrt(jnp.mean(jnp.square(hidden_f), axis=1, keepdims=True) + 1e-05)
    w_ext = jnp.concatenate([w_shard, g_shard[None, :]], axis=0)
    gathered = lax.all_gather(w_ext, "fsdp", axis=0, tiled=False)
    w_full = gathered[:, :rows, :].reshape(-1, heads)
    g_full = gathered[:, rows, :].reshape(-1)
    xhat = hidden_f * ratio
    normed = (xhat * g_full.astype(jnp.float32)[None, :]).astype(jnp.bfloat16)
    values = jnp.dot(normed, w_full, preferred_element_type=jnp.float32) * scale
    delta = (values - goal.astype(jnp.float32)).astype(jnp.bfloat16)

    local_hidden = lax.all_to_all(token_batch, "fsdp", 1, 0, tiled=True)
    local_ratio = lax.all_gather(ratio, "fsdp", axis=0, tiled=True)
    local_delta = lax.all_gather(delta, "fsdp", axis=0, tiled=True)
    local_xhat = local_hidden.astype(jnp.float32) * local_ratio
    g_f = g_shard.astype(jnp.float32)
    local_normed = (local_xhat * g_f[None, :]).astype(jnp.bfloat16)
    sq_normed = jnp.square(local_normed.astype(jnp.float32)).astype(jnp.bfloat16)
    sq_delta = jnp.square(local_delta.astype(jnp.float32)).astype(jnp.bfloat16)
    fisher = jnp.einsum("td,th->dh", sq_normed, sq_delta, preferred_element_type=jnp.float32)
    back = jnp.einsum("th,dh->td", local_delta, w_shard, preferred_element_type=jnp.float32) * scale
    gain_info = jnp.sum(jnp.square(back * local_xhat), axis=0)

    extra = jnp.zeros((rows, 128), jnp.float32)
    extra = extra.at[:, 0].set(gain_info * g_f).at[:, 1].set(gain_info)
    pack = jnp.concatenate([fisher * w_shard.astype(jnp.float32), fisher, extra], axis=1)
    cols = pack.shape[1]
    piece = rows // (n_t * n_dp)
    pack = pack.reshape(n_dp, n_t, piece, cols).transpose(1, 0, 2, 3).reshape(n_t * n_dp, piece, cols)
    parts = lax.all_to_all(pack, ("template", "dp"), 0, 0, tiled=True)
    total = jnp.sum(parts, axis=0, keepdims=True)
    spread = lax.all_to_all(jnp.broadcast_to(total, (n_t, piece, cols)), "template", 0, 0, tiled=True)
    full = spread.reshape(n_t * piece, cols)
    merged = full[:, :heads] / full[:, heads : 2 * heads]
    merged_gain = full[:, 2 * heads] / full[:, 2 * heads + 1]
    return merged, merged_gain


def solution(mesh):
    in_specs = (
        P("template", ("fsdp", "dp"), None),
        P("template", ("fsdp", "dp"), None),
        P("template", "fsdp", None),
        P("template", "fsdp"),
    )
    out_specs = (P(("fsdp", "dp"), None), P(("fsdp", "dp")))
    return jax.shard_map(body, mesh=mesh, in_specs=in_specs, out_specs=out_specs, check_vma=False)
```

```python
import math

import jax
import jax.numpy as jnp
from jax import lax
from jax.sharding import PartitionSpec as P


def body(hidden, target, weight, gain):
    token_batch = hidden[0]
    goal = target[0]
    w_shard = weight[0]
    g_shard = gain[0]
    width = token_batch.shape[1]
    rows = w_shard.shape[0]
    heads = w_shard.shape[1]
    scale = 1.0 / math.sqrt(width)
    n_t = lax.axis_size("template")
    n_dp = lax.axis_size("dp")

    hidden_f = token_batch.astype(jnp.float32)
    ratio = lax.rsqrt(jnp.mean(jnp.square(hidden_f), axis=1, keepdims=True) + 1e-05)
    swap = [(i, (i + 1) % n_dp) for i in range(n_dp)]
    other_hidden = lax.ppermute(token_batch, "dp", swap)
    other_ratio = lax.ppermute(ratio, "dp", swap)
    half = heads // n_dp
    dp_at = lax.axis_index("dp")
    w_cols = lax.dynamic_slice_in_dim(w_shard, dp_at * half, half, 1)
    w_ext = jnp.concatenate([w_cols, g_shard.reshape(-1, half)], axis=0)
    gathered = lax.all_gather(w_ext, "fsdp", axis=0, tiled=False)
    w_half = gathered[:, :rows, :].reshape(-1, half)
    g_full = gathered[:, rows:, :].reshape(-1).astype(jnp.float32)
    xhat = hidden_f * ratio
    normed = (xhat * g_full[None, :]).astype(jnp.bfloat16)
    other_normed = (other_hidden.astype(jnp.float32) * other_ratio * g_full[None, :]).astype(jnp.bfloat16)
    mine_half = jnp.dot(normed, w_half, preferred_element_type=jnp.float32)
    theirs_half = jnp.dot(other_normed, w_half, preferred_element_type=jnp.float32)
    from_other = lax.ppermute(theirs_half, "dp", swap)
    both = jnp.stack([mine_half, from_other])
    first = jnp.where(dp_at == 0, both[0], both[1])
    second = jnp.where(dp_at == 0, both[1], both[0])
    values = jnp.concatenate([first, second], axis=1) * scale
    delta = (values - goal.astype(jnp.float32)).astype(jnp.bfloat16)

    local_hidden = lax.all_to_all(token_batch, "fsdp", 1, 0, tiled=True)
    local_ratio = lax.all_gather(ratio, "fsdp", axis=0, tiled=True)
    local_delta = lax.all_gather(delta, "fsdp", axis=0, tiled=True)
    local_xhat = local_hidden.astype(jnp.float32) * local_ratio
    g_f = g_shard.astype(jnp.float32)
    local_normed = (local_xhat * g_f[None, :]).astype(jnp.bfloat16)
    sq_normed = jnp.square(local_normed.astype(jnp.float32)).astype(jnp.bfloat16)
    sq_delta = jnp.square(local_delta.astype(jnp.float32)).astype(jnp.bfloat16)
    fisher = jnp.einsum("td,th->dh", sq_normed, sq_delta, preferred_element_type=jnp.float32)
    back = jnp.einsum("th,dh->td", local_delta, w_shard, preferred_element_type=jnp.float32) * scale
    gain_info = jnp.sum(jnp.square(back * local_xhat), axis=0)

    extra = jnp.zeros((rows, 128), jnp.float32)
    extra = extra.at[:, 0].set(gain_info * g_f).at[:, 1].set(gain_info)
    pack = jnp.concatenate([fisher * w_shard.astype(jnp.float32), fisher, extra], axis=1)
    cols = pack.shape[1]
    piece = rows // (n_t * n_dp)
    pack = pack.reshape(n_dp, n_t, piece, cols).transpose(1, 0, 2, 3).reshape(n_t * n_dp, piece, cols)
    parts = lax.all_to_all(pack, ("template", "dp"), 0, 0, tiled=True)
    total = jnp.sum(parts, axis=0, keepdims=True)
    spread = lax.all_to_all(jnp.broadcast_to(total, (n_t, piece, cols)), "template", 0, 0, tiled=True)
    full = spread.reshape(n_t * piece, cols)
    merged = full[:, :heads] / full[:, heads : 2 * heads]
    merged_gain = full[:, 2 * heads] / full[:, 2 * heads + 1]
    return merged, merged_gain


def solution(mesh):
    in_specs = (
        P("template", ("fsdp", "dp"), None),
        P("template", ("fsdp", "dp"), None),
        P("template", "fsdp", None),
        P("template", "fsdp"),
    )
    out_specs = (P(("fsdp", "dp"), None), P(("fsdp", "dp")))
    return jax.shard_map(body, mesh=mesh, in_specs=in_specs, out_specs=out_specs, check_vma=False)
```

```python
import math

import jax
import jax.numpy as jnp
from jax import lax
from jax.sharding import PartitionSpec as P


def body(hidden, target, weight, gain):
    token_batch = hidden[0]
    goal = target[0]
    w_shard = weight[0]
    g_shard = gain[0]
    width = token_batch.shape[1]
    rows = w_shard.shape[0]
    heads = w_shard.shape[1]
    scale = 1.0 / math.sqrt(width)
    n_t = lax.axis_size("template")
    n_dp = lax.axis_size("dp")

    hidden_f = token_batch.astype(jnp.float32)
    ratio = lax.rsqrt(jnp.mean(jnp.square(hidden_f), axis=1, keepdims=True) + 1e-05)
    swap = [(i, (i + 1) % n_dp) for i in range(n_dp)]
    other_hidden = lax.ppermute(token_batch, "dp", swap)
    other_ratio = lax.ppermute(ratio, "dp", swap)
    half = heads // n_dp
    dp_at = lax.axis_index("dp")
    w_cols = lax.dynamic_slice_in_dim(w_shard, dp_at * half, half, 1)
    w_ext = jnp.concatenate([w_cols, g_shard.reshape(-1, half)], axis=0)
    gathered = lax.all_gather(w_ext, "fsdp", axis=0, tiled=False)
    w_half = gathered[:, :rows, :].reshape(-1, half)
    g_full = gathered[:, rows:, :].reshape(-1).astype(jnp.float32)
    xhat = hidden_f * ratio
    normed = (xhat * g_full[None, :]).astype(jnp.bfloat16)
    other_normed = (other_hidden.astype(jnp.float32) * other_ratio * g_full[None, :]).astype(jnp.bfloat16)
    mine_half = jnp.dot(normed, w_half, preferred_element_type=jnp.float32)
    theirs_half = jnp.dot(other_normed, w_half, preferred_element_type=jnp.float32)
    from_other = lax.ppermute(theirs_half, "dp", swap)
    both = jnp.stack([mine_half, from_other])
    first = jnp.where(dp_at == 0, both[0], both[1])
    second = jnp.where(dp_at == 0, both[1], both[0])
    values = jnp.concatenate([first, second], axis=1) * scale
    delta = (values - goal.astype(jnp.float32)).astype(jnp.bfloat16)

    local_hidden = lax.all_to_all(token_batch, "fsdp", 1, 0, tiled=True)
    local_ratio = lax.all_gather(ratio, "fsdp", axis=0, tiled=True)
    local_xhat = local_hidden.astype(jnp.float32) * local_ratio
    g_f = g_shard.astype(jnp.float32)
    local_normed = (local_xhat * g_f[None, :]).astype(jnp.bfloat16)
    sq_normed = jnp.square(local_normed.astype(jnp.float32)).astype(jnp.bfloat16)
    w_f = w_shard.astype(jnp.float32)
    piece = rows // (n_t * n_dp)

    def reduce_rows(pack):
        cols = pack.shape[1]
        pack = pack.reshape(n_dp, n_t, piece, cols).transpose(1, 0, 2, 3).reshape(n_t * n_dp, piece, cols)
        parts = lax.all_to_all(pack, ("template", "dp"), 0, 0, tiled=True)
        total = jnp.sum(parts, axis=0, keepdims=True)
        spread = lax.all_to_all(jnp.broadcast_to(total, (n_t, piece, cols)), "template", 0, 0, tiled=True)
        return spread.reshape(n_t * piece, cols)

    delta_a = lax.all_gather(delta[:, :half], "fsdp", axis=0, tiled=True)
    delta_b = lax.all_gather(delta[:, half:], "fsdp", axis=0, tiled=True)
    sq_a = jnp.square(delta_a.astype(jnp.float32)).astype(jnp.bfloat16)
    fisher_a = jnp.einsum("td,th->dh", sq_normed, sq_a, preferred_element_type=jnp.float32)
    full_a = reduce_rows(jnp.concatenate([fisher_a * w_f[:, :half], fisher_a], axis=1))
    full_a, sq_normed, local_xhat = lax.optimization_barrier((full_a, sq_normed, local_xhat))
    sq_b = jnp.square(delta_b.astype(jnp.float32)).astype(jnp.bfloat16)
    fisher_b = jnp.einsum("td,th->dh", sq_normed, sq_b, preferred_element_type=jnp.float32)
    local_delta = jnp.concatenate([delta_a, delta_b], axis=1)
    back = jnp.einsum("th,dh->td", local_delta, w_shard, preferred_element_type=jnp.float32) * scale
    gain_info = jnp.sum(jnp.square(back * local_xhat), axis=0)
    extra = jnp.zeros((rows, 128), jnp.float32)
    extra = extra.at[:, 0].set(gain_info * g_f).at[:, 1].set(gain_info)
    full_b = reduce_rows(jnp.concatenate([fisher_b * w_f[:, half:], fisher_b, extra], axis=1))
    merged = jnp.concatenate(
        [full_a[:, :half] / full_a[:, half:], full_b[:, :half] / full_b[:, half : 2 * half]], axis=1
    )
    merged_gain = full_b[:, 2 * half] / full_b[:, 2 * half + 1]
    return merged, merged_gain


def solution(mesh):
    in_specs = (
        P("template", ("fsdp", "dp"), None),
        P("template", ("fsdp", "dp"), None),
        P("template", "fsdp", None),
        P("template", "fsdp"),
    )
    out_specs = (P(("fsdp", "dp"), None), P(("fsdp", "dp")))
    return jax.shard_map(body, mesh=mesh, in_specs=in_specs, out_specs=out_specs, check_vma=False)
```

```python
import math

import jax
import jax.numpy as jnp
from jax import lax
from jax.sharding import PartitionSpec as P


def body(hidden, target, weight, gain):
    token_batch = hidden[0]
    goal = target[0]
    w_shard = weight[0]
    g_shard = gain[0]
    width = token_batch.shape[1]
    rows = w_shard.shape[0]
    heads = w_shard.shape[1]
    scale = 1.0 / math.sqrt(width)
    n_t = lax.axis_size("template")
    n_dp = lax.axis_size("dp")

    hidden_f = token_batch.astype(jnp.float32)
    ratio = lax.rsqrt(jnp.mean(jnp.square(hidden_f), axis=1, keepdims=True) + 1e-05)
    swap = [(i, (i + 1) % n_dp) for i in range(n_dp)]
    other_hidden = lax.ppermute(token_batch, "dp", swap)
    other_ratio = lax.ppermute(ratio, "dp", swap)
    half = heads // n_dp
    dp_at = lax.axis_index("dp")
    w_cols = lax.dynamic_slice_in_dim(w_shard, dp_at * half, half, 1)
    w_ext = jnp.concatenate([w_cols, g_shard.reshape(-1, half)], axis=0)
    gathered = lax.all_gather(w_ext, "fsdp", axis=0, tiled=False)
    w_half = gathered[:, :rows, :].reshape(-1, half)
    g_full = gathered[:, rows:, :].reshape(-1).astype(jnp.float32)
    xhat = hidden_f * ratio
    normed = (xhat * g_full[None, :]).astype(jnp.bfloat16)
    other_normed = (other_hidden.astype(jnp.float32) * other_ratio * g_full[None, :]).astype(jnp.bfloat16)
    mine_half = jnp.dot(normed, w_half, preferred_element_type=jnp.float32)
    theirs_half = jnp.dot(other_normed, w_half, preferred_element_type=jnp.float32)
    from_other = lax.ppermute(theirs_half, "dp", swap)
    both = jnp.stack([mine_half, from_other])
    first = jnp.where(dp_at == 0, both[0], both[1])
    second = jnp.where(dp_at == 0, both[1], both[0])
    values = jnp.concatenate([first, second], axis=1) * scale
    delta = (values - goal.astype(jnp.float32)).astype(jnp.bfloat16)

    late_batch, _ = lax.optimization_barrier((token_batch, delta))
    local_hidden = lax.all_to_all(late_batch, "fsdp", 1, 0, tiled=True)
    local_ratio = lax.all_gather(ratio, "fsdp", axis=0, tiled=True)
    local_delta = lax.all_gather(delta, "fsdp", axis=0, tiled=True)
    local_xhat = local_hidden.astype(jnp.float32) * local_ratio
    g_f = g_shard.astype(jnp.float32)
    local_normed = (local_xhat * g_f[None, :]).astype(jnp.bfloat16)
    sq_normed = jnp.square(local_normed.astype(jnp.float32)).astype(jnp.bfloat16)
    sq_delta = jnp.square(local_delta.astype(jnp.float32)).astype(jnp.bfloat16)
    fisher = jnp.einsum("td,th->dh", sq_normed, sq_delta, preferred_element_type=jnp.float32)
    back = jnp.einsum("th,dh->td", local_delta, w_shard, preferred_element_type=jnp.float32) * scale
    gain_info = jnp.sum(jnp.square(back * local_xhat), axis=0)

    extra = jnp.zeros((rows, 128), jnp.float32)
    extra = extra.at[:, 0].set(gain_info * g_f).at[:, 1].set(gain_info)
    pack = jnp.concatenate([fisher * w_shard.astype(jnp.float32), fisher, extra], axis=1)
    cols = pack.shape[1]
    piece = rows // (n_t * n_dp)
    pack = pack.reshape(n_dp, n_t, piece, cols).transpose(1, 0, 2, 3).reshape(n_t * n_dp, piece, cols)
    parts = lax.all_to_all(pack, ("template", "dp"), 0, 0, tiled=True)
    total = jnp.sum(parts, axis=0, keepdims=True)
    spread = lax.all_to_all(jnp.broadcast_to(total, (n_t, piece, cols)), "template", 0, 0, tiled=True)
    full = spread.reshape(n_t * piece, cols)
    merged = full[:, :heads] / full[:, heads : 2 * heads]
    merged_gain = full[:, 2 * heads] / full[:, 2 * heads + 1]
    return merged, merged_gain


def solution(mesh):
    in_specs = (
        P("template", ("fsdp", "dp"), None),
        P("template", ("fsdp", "dp"), None),
        P("template", "fsdp", None),
        P("template", "fsdp"),
    )
    out_specs = (P(("fsdp", "dp"), None), P(("fsdp", "dp")))
    return jax.shard_map(body, mesh=mesh, in_specs=in_specs, out_specs=out_specs, check_vma=False)
```

```python
import math

import jax
import jax.numpy as jnp
from jax import lax
from jax.sharding import PartitionSpec as P


def body(hidden, target, weight, gain):
    token_batch = hidden[0]
    goal = target[0]
    w_shard = weight[0]
    g_shard = gain[0]
    width = token_batch.shape[1]
    rows = w_shard.shape[0]
    heads = w_shard.shape[1]
    scale = 1.0 / math.sqrt(width)
    n_t = lax.axis_size("template")
    n_dp = lax.axis_size("dp")

    hidden_f = token_batch.astype(jnp.float32)
    ratio = lax.rsqrt(jnp.mean(jnp.square(hidden_f), axis=1, keepdims=True) + 1e-05)
    swap = [(i, (i + 1) % n_dp) for i in range(n_dp)]
    other_hidden = lax.ppermute(token_batch, "dp", swap)
    other_ratio = lax.ppermute(ratio, "dp", swap)
    half = heads // n_dp
    dp_at = lax.axis_index("dp")
    w_cols = lax.dynamic_slice_in_dim(w_shard, dp_at * half, half, 1)
    w_ext = jnp.concatenate([w_cols, g_shard.reshape(-1, half)], axis=0)
    gathered = lax.all_gather(w_ext, "fsdp", axis=0, tiled=False)
    w_half = gathered[:, :rows, :].reshape(-1, half)
    g_full = gathered[:, rows:, :].reshape(-1).astype(jnp.float32)
    xhat = hidden_f * ratio
    normed = (xhat * g_full[None, :]).astype(jnp.bfloat16)
    other_normed = (other_hidden.astype(jnp.float32) * other_ratio * g_full[None, :]).astype(jnp.bfloat16)
    mine_half = jnp.dot(normed, w_half, preferred_element_type=jnp.float32)
    theirs_half = jnp.dot(other_normed, w_half, preferred_element_type=jnp.float32)
    from_other = lax.ppermute(theirs_half, "dp", swap)
    both = jnp.stack([mine_half, from_other])
    first = jnp.where(dp_at == 0, both[0], both[1])
    second = jnp.where(dp_at == 0, both[1], both[0])
    values = jnp.concatenate([first, second], axis=1) * scale
    delta = (values - goal.astype(jnp.float32)).astype(jnp.bfloat16)

    late_batch, _, _ = lax.optimization_barrier((token_batch, mine_half, other_hidden))
    local_hidden = lax.all_to_all(late_batch, "fsdp", 1, 0, tiled=True)
    local_ratio = lax.all_gather(ratio, "fsdp", axis=0, tiled=True)
    local_delta = lax.all_gather(delta, "fsdp", axis=0, tiled=True)
    local_xhat = local_hidden.astype(jnp.float32) * local_ratio
    g_f = g_shard.astype(jnp.float32)
    local_normed = (local_xhat * g_f[None, :]).astype(jnp.bfloat16)
    sq_normed = jnp.square(local_normed.astype(jnp.float32)).astype(jnp.bfloat16)
    sq_delta = jnp.square(local_delta.astype(jnp.float32)).astype(jnp.bfloat16)
    fisher = jnp.einsum("td,th->dh", sq_normed, sq_delta, preferred_element_type=jnp.float32)
    back = jnp.einsum("th,dh->td", local_delta, w_shard, preferred_element_type=jnp.float32) * scale
    gain_info = jnp.sum(jnp.square(back * local_xhat), axis=0)

    extra = jnp.zeros((rows, 128), jnp.float32)
    extra = extra.at[:, 0].set(gain_info * g_f).at[:, 1].set(gain_info)
    pack = jnp.concatenate([fisher * w_shard.astype(jnp.float32), fisher, extra], axis=1)
    cols = pack.shape[1]
    piece = rows // (n_t * n_dp)
    pack = pack.reshape(n_dp, n_t, piece, cols).transpose(1, 0, 2, 3).reshape(n_t * n_dp, piece, cols)
    parts = lax.all_to_all(pack, ("template", "dp"), 0, 0, tiled=True)
    total = jnp.sum(parts, axis=0, keepdims=True)
    spread = lax.all_to_all(jnp.broadcast_to(total, (n_t, piece, cols)), "template", 0, 0, tiled=True)
    full = spread.reshape(n_t * piece, cols)
    merged = full[:, :heads] / full[:, heads : 2 * heads]
    merged_gain = full[:, 2 * heads] / full[:, 2 * heads + 1]
    return merged, merged_gain


def solution(mesh):
    in_specs = (
        P("template", ("fsdp", "dp"), None),
        P("template", ("fsdp", "dp"), None),
        P("template", "fsdp", None),
        P("template", "fsdp"),
    )
    out_specs = (P(("fsdp", "dp"), None), P(("fsdp", "dp")))
    return jax.shard_map(body, mesh=mesh, in_specs=in_specs, out_specs=out_specs, check_vma=False)
```

```python
import math

import jax
import jax.numpy as jnp
from jax import lax
from jax.sharding import PartitionSpec as P


def body(hidden, target, weight, gain):
    token_batch = hidden[0]
    goal = target[0]
    w_shard = weight[0]
    g_shard = gain[0]
    width = token_batch.shape[1]
    rows = w_shard.shape[0]
    heads = w_shard.shape[1]
    scale = 1.0 / math.sqrt(width)
    n_t = lax.axis_size("template")
    n_dp = lax.axis_size("dp")

    hidden_f = token_batch.astype(jnp.float32)
    ratio = lax.rsqrt(jnp.mean(jnp.square(hidden_f), axis=1, keepdims=True) + 1e-05)
    swap = [(i, (i + 1) % n_dp) for i in range(n_dp)]
    other_hidden = lax.ppermute(token_batch, "dp", swap)
    other_f = other_hidden.astype(jnp.float32)
    other_ratio = lax.rsqrt(jnp.mean(jnp.square(other_f), axis=1, keepdims=True) + 1e-05)
    half = heads // n_dp
    dp_at = lax.axis_index("dp")
    w_cols = lax.dynamic_slice_in_dim(w_shard, dp_at * half, half, 1)
    w_ext = jnp.concatenate([w_cols, g_shard.reshape(-1, half)], axis=0)
    gathered = lax.all_gather(w_ext, "fsdp", axis=0, tiled=False)
    w_half = gathered[:, :rows, :].reshape(-1, half)
    g_full = gathered[:, rows:, :].reshape(-1).astype(jnp.float32)
    xhat = hidden_f * ratio
    normed = (xhat * g_full[None, :]).astype(jnp.bfloat16)
    other_normed = (other_f * other_ratio * g_full[None, :]).astype(jnp.bfloat16)
    mine_half = jnp.dot(normed, w_half, preferred_element_type=jnp.float32)
    theirs_half = jnp.dot(other_normed, w_half, preferred_element_type=jnp.float32)
    from_other = lax.ppermute(theirs_half, "dp", swap)
    both = jnp.stack([mine_half, from_other])
    first = jnp.where(dp_at == 0, both[0], both[1])
    second = jnp.where(dp_at == 0, both[1], both[0])
    values = jnp.concatenate([first, second], axis=1) * scale
    delta = (values - goal.astype(jnp.float32)).astype(jnp.bfloat16)

    late_batch, _, _ = lax.optimization_barrier((token_batch, mine_half, other_normed))
    local_hidden = lax.all_to_all(late_batch, "fsdp", 1, 0, tiled=True)
    local_ratio = lax.all_gather(ratio, "fsdp", axis=0, tiled=True)
    local_delta = lax.all_gather(delta, "fsdp", axis=0, tiled=True)
    local_xhat = local_hidden.astype(jnp.float32) * local_ratio
    g_f = g_shard.astype(jnp.float32)
    local_normed = (local_xhat * g_f[None, :]).astype(jnp.bfloat16)
    sq_normed = jnp.square(local_normed.astype(jnp.float32)).astype(jnp.bfloat16)
    sq_delta = jnp.square(local_delta.astype(jnp.float32)).astype(jnp.bfloat16)
    fisher = jnp.einsum("td,th->dh", sq_normed, sq_delta, preferred_element_type=jnp.float32)
    back = jnp.einsum("th,dh->td", local_delta, w_shard, preferred_element_type=jnp.float32) * scale
    gain_info = jnp.sum(jnp.square(back * local_xhat), axis=0)

    extra = jnp.zeros((rows, 128), jnp.float32)
    extra = extra.at[:, 0].set(gain_info * g_f).at[:, 1].set(gain_info)
    pack = jnp.concatenate([fisher * w_shard.astype(jnp.float32), fisher, extra], axis=1)
    cols = pack.shape[1]
    piece = rows // (n_t * n_dp)
    pack = pack.reshape(n_t * n_dp, piece, cols)
    parts = lax.all_to_all(pack, ("dp", "template"), 0, 0, tiled=True)
    total = jnp.sum(parts, axis=0, keepdims=True)
    spread = lax.all_to_all(jnp.broadcast_to(total, (n_t, piece, cols)), "template", 0, 0, tiled=True)
    full = spread.reshape(n_t * piece, cols)
    merged = full[:, :heads] / full[:, heads : 2 * heads]
    merged_gain = full[:, 2 * heads] / full[:, 2 * heads + 1]
    return merged, merged_gain


def solution(mesh):
    in_specs = (
        P("template", ("fsdp", "dp"), None),
        P("template", ("fsdp", "dp"), None),
        P("template", "fsdp", None),
        P("template", "fsdp"),
    )
    out_specs = (P(("fsdp", "dp"), None), P(("fsdp", "dp")))
    return jax.shard_map(body, mesh=mesh, in_specs=in_specs, out_specs=out_specs, check_vma=False)
```

```python
import math

import jax
import jax.numpy as jnp
from jax import lax
from jax.sharding import PartitionSpec as P


def body(hidden, target, weight, gain):
    token_batch = hidden[0]
    goal = target[0]
    w_shard = weight[0]
    g_shard = gain[0]
    width = token_batch.shape[1]
    rows = w_shard.shape[0]
    heads = w_shard.shape[1]
    scale = 1.0 / math.sqrt(width)
    n_t = lax.axis_size("template")
    n_dp = lax.axis_size("dp")

    hidden_f = token_batch.astype(jnp.float32)
    ratio = lax.rsqrt(jnp.mean(jnp.square(hidden_f), axis=1, keepdims=True) + 1e-05)
    swap = [(i, (i + 1) % n_dp) for i in range(n_dp)]
    other_hidden = lax.ppermute(token_batch, "dp", swap)
    other_f = other_hidden.astype(jnp.float32)
    other_ratio = lax.rsqrt(jnp.mean(jnp.square(other_f), axis=1, keepdims=True) + 1e-05)
    half = heads // n_dp
    dp_at = lax.axis_index("dp")
    w_cols = lax.dynamic_slice_in_dim(w_shard, dp_at * half, half, 1)
    w_ext = jnp.concatenate([w_cols, g_shard.reshape(-1, half)], axis=0)
    gathered = lax.all_gather(w_ext, "fsdp", axis=0, tiled=False)
    w_half = gathered[:, :rows, :].reshape(-1, half)
    g_full = gathered[:, rows:, :].reshape(-1).astype(jnp.float32)
    xhat = hidden_f * ratio
    normed = (xhat * g_full[None, :]).astype(jnp.bfloat16)
    other_normed = (other_f * other_ratio * g_full[None, :]).astype(jnp.bfloat16)
    mine_half = jnp.dot(normed, w_half, preferred_element_type=jnp.float32)
    theirs_half = jnp.dot(other_normed, w_half, preferred_element_type=jnp.float32)
    from_other = lax.ppermute(theirs_half, "dp", swap)
    both = jnp.stack([mine_half, from_other])
    first = jnp.where(dp_at == 0, both[0], both[1])
    second = jnp.where(dp_at == 0, both[1], both[0])
    values = jnp.concatenate([first, second], axis=1) * scale
    delta = (values - goal.astype(jnp.float32)).astype(jnp.bfloat16)

    late_batch, _, _ = lax.optimization_barrier((token_batch, mine_half, other_normed))
    local_hidden = lax.all_to_all(late_batch, "fsdp", 1, 0, tiled=True)
    local_ratio = lax.all_gather(ratio, "fsdp", axis=0, tiled=True)
    local_delta = lax.all_gather(delta, "fsdp", axis=0, tiled=True)
    local_xhat = local_hidden.astype(jnp.float32) * local_ratio
    g_f = g_shard.astype(jnp.float32)
    local_normed = (local_xhat * g_f[None, :]).astype(jnp.bfloat16)
    sq_normed = jnp.square(local_normed.astype(jnp.float32)).astype(jnp.bfloat16)
    sq_delta = jnp.square(local_delta.astype(jnp.float32)).astype(jnp.bfloat16)
    fisher = jnp.einsum("td,th->dh", sq_normed, sq_delta, preferred_element_type=jnp.float32)
    back = jnp.einsum("th,dh->td", local_delta, w_shard, preferred_element_type=jnp.float32) * scale
    gain_info = jnp.sum(jnp.square(back * local_xhat), axis=0)

    extra = jnp.zeros((rows, 128), jnp.float32)
    extra = extra.at[:, 0].set(gain_info * g_f).at[:, 1].set(gain_info)
    pack = jnp.concatenate([fisher * w_shard.astype(jnp.float32), fisher, extra], axis=1)
    cols = pack.shape[1]
    piece = rows // (n_t * n_dp)
    pack = pack.reshape(n_t * n_dp, piece, cols)
    parts = lax.all_to_all(pack, ("dp", "template"), 0, 0, tiled=True)
    total = jnp.sum(parts, axis=0)
    ratio_block = jnp.zeros((piece, 128), jnp.float32).at[:, 0].set(total[:, 2 * heads] / total[:, 2 * heads + 1])
    done = jnp.concatenate([total[:, :heads] / total[:, heads : 2 * heads], ratio_block], axis=1)
    spread = lax.all_to_all(jnp.broadcast_to(done[None], (n_t,) + done.shape), "template", 0, 0, tiled=True)
    full = spread.reshape(n_t * piece, done.shape[1])
    merged = full[:, :heads]
    merged_gain = full[:, heads]
    return merged, merged_gain


def solution(mesh):
    in_specs = (
        P("template", ("fsdp", "dp"), None),
        P("template", ("fsdp", "dp"), None),
        P("template", "fsdp", None),
        P("template", "fsdp"),
    )
    out_specs = (P(("fsdp", "dp"), None), P(("fsdp", "dp")))
    return jax.shard_map(body, mesh=mesh, in_specs=in_specs, out_specs=out_specs, check_vma=False)
```

```python
import math

import jax
import jax.numpy as jnp
from jax import lax
from jax.sharding import PartitionSpec as P


def body(hidden, target, weight, gain):
    token_batch = hidden[0]
    goal = target[0]
    w_shard = weight[0]
    g_shard = gain[0]
    width = token_batch.shape[1]
    rows = w_shard.shape[0]
    heads = w_shard.shape[1]
    scale = 1.0 / math.sqrt(width)
    n_t = lax.axis_size("template")
    n_dp = lax.axis_size("dp")

    hidden_f = token_batch.astype(jnp.float32)
    ratio = lax.rsqrt(jnp.mean(jnp.square(hidden_f), axis=1, keepdims=True) + 1e-05)
    swap = [(i, (i + 1) % n_dp) for i in range(n_dp)]
    other_hidden = lax.ppermute(token_batch, "dp", swap)
    other_f = other_hidden.astype(jnp.float32)
    other_ratio = lax.rsqrt(jnp.mean(jnp.square(other_f), axis=1, keepdims=True) + 1e-05)
    half = heads // n_dp
    dp_at = lax.axis_index("dp")
    w_cols = lax.dynamic_slice_in_dim(w_shard, dp_at * half, half, 1)
    w_ext = jnp.concatenate([w_cols, g_shard.reshape(-1, half)], axis=0)
    gathered = lax.all_gather(w_ext, "fsdp", axis=0, tiled=False)
    w_half = gathered[:, :rows, :].reshape(-1, half)
    g_full = gathered[:, rows:, :].reshape(-1).astype(jnp.float32)
    xhat = hidden_f * ratio
    normed = (xhat * g_full[None, :]).astype(jnp.bfloat16)
    other_normed = (other_f * other_ratio * g_full[None, :]).astype(jnp.bfloat16)
    mine_half = jnp.dot(normed, w_half, preferred_element_type=jnp.float32)
    theirs_half = jnp.dot(other_normed, w_half, preferred_element_type=jnp.float32)
    from_other = lax.ppermute(theirs_half, "dp", swap)
    both = jnp.stack([mine_half, from_other])
    first = jnp.where(dp_at == 0, both[0], both[1])
    second = jnp.where(dp_at == 0, both[1], both[0])
    values = jnp.concatenate([first, second], axis=1) * scale
    delta = (values - goal.astype(jnp.float32)).astype(jnp.bfloat16)

    late_batch, _, _ = lax.optimization_barrier((token_batch, mine_half, other_normed))
    n_f = lax.axis_size("fsdp")
    early_rows = rows // 4
    by_dest = token_batch.reshape(token_batch.shape[0], n_f, rows)
    early_hidden = lax.all_to_all(by_dest[:, :, :early_rows], "fsdp", 1, 0, tiled=True)
    late_dest = late_batch.reshape(token_batch.shape[0], n_f, rows)
    late_hidden = lax.all_to_all(late_dest[:, :, early_rows:], "fsdp", 1, 0, tiled=True)
    local_hidden = jnp.concatenate(
        [early_hidden.reshape(-1, early_rows), late_hidden.reshape(-1, rows - early_rows)], axis=1
    )
    local_ratio = lax.all_gather(ratio, "fsdp", axis=0, tiled=True)
    local_delta = lax.all_gather(delta, "fsdp", axis=0, tiled=True)
    local_xhat = local_hidden.astype(jnp.float32) * local_ratio
    g_f = g_shard.astype(jnp.float32)
    local_normed = (local_xhat * g_f[None, :]).astype(jnp.bfloat16)
    sq_normed = jnp.square(local_normed.astype(jnp.float32)).astype(jnp.bfloat16)
    sq_delta = jnp.square(local_delta.astype(jnp.float32)).astype(jnp.bfloat16)
    fisher = jnp.einsum("td,th->dh", sq_normed, sq_delta, preferred_element_type=jnp.float32)
    back = jnp.einsum("th,dh->td", local_delta, w_shard, preferred_element_type=jnp.float32) * scale
    gain_info = jnp.sum(jnp.square(back * local_xhat), axis=0)

    extra = jnp.zeros((rows, 128), jnp.float32)
    extra = extra.at[:, 0].set(gain_info * g_f).at[:, 1].set(gain_info)
    pack = jnp.concatenate([fisher * w_shard.astype(jnp.float32), fisher, extra], axis=1)
    cols = pack.shape[1]
    piece = rows // (n_t * n_dp)
    pack = pack.reshape(n_t * n_dp, piece, cols)
    parts = lax.all_to_all(pack, ("dp", "template"), 0, 0, tiled=True)
    total = jnp.sum(parts, axis=0)
    ratio_block = jnp.zeros((piece, 128), jnp.float32).at[:, 0].set(total[:, 2 * heads] / total[:, 2 * heads + 1])
    done = jnp.concatenate([total[:, :heads] / total[:, heads : 2 * heads], ratio_block], axis=1)
    spread = lax.all_to_all(jnp.broadcast_to(done[None], (n_t,) + done.shape), "template", 0, 0, tiled=True)
    full = spread.reshape(n_t * piece, done.shape[1])
    merged = full[:, :heads]
    merged_gain = full[:, heads]
    return merged, merged_gain


def solution(mesh):
    in_specs = (
        P("template", ("fsdp", "dp"), None),
        P("template", ("fsdp", "dp"), None),
        P("template", "fsdp", None),
        P("template", "fsdp"),
    )
    out_specs = (P(("fsdp", "dp"), None), P(("fsdp", "dp")))
    return jax.shard_map(body, mesh=mesh, in_specs=in_specs, out_specs=out_specs, check_vma=False)
```

```python
import math

import jax
import jax.numpy as jnp
from jax import lax
from jax.sharding import PartitionSpec as P


def body(hidden, target, weight, gain):
    token_batch = hidden[0]
    goal = target[0]
    w_shard = weight[0]
    g_shard = gain[0]
    width = token_batch.shape[1]
    rows = w_shard.shape[0]
    heads = w_shard.shape[1]
    scale = 1.0 / math.sqrt(width)
    n_t = lax.axis_size("template")
    n_dp = lax.axis_size("dp")

    hidden_f = token_batch.astype(jnp.float32)
    ratio = lax.rsqrt(jnp.mean(jnp.square(hidden_f), axis=1, keepdims=True) + 1e-05)
    swap = [(i, (i + 1) % n_dp) for i in range(n_dp)]
    other_hidden = lax.ppermute(token_batch, "dp", swap)
    other_f = other_hidden.astype(jnp.float32)
    other_ratio = lax.rsqrt(jnp.mean(jnp.square(other_f), axis=1, keepdims=True) + 1e-05)
    half = heads // n_dp
    dp_at = lax.axis_index("dp")
    w_cols = lax.dynamic_slice_in_dim(w_shard, dp_at * half, half, 1)
    w_ext = jnp.concatenate([w_cols, g_shard.reshape(-1, half)], axis=0)
    gathered = lax.all_gather(w_ext, "fsdp", axis=0, tiled=False)
    w_half = gathered[:, :rows, :].reshape(-1, half)
    g_full = gathered[:, rows:, :].reshape(-1).astype(jnp.float32)
    xhat = hidden_f * ratio
    normed = (xhat * g_full[None, :]).astype(jnp.bfloat16)
    other_normed = (other_f * other_ratio * g_full[None, :]).astype(jnp.bfloat16)
    mine_half = jnp.dot(normed, w_half, preferred_element_type=jnp.float32)
    theirs_half = jnp.dot(other_normed, w_half, preferred_element_type=jnp.float32)
    from_other = lax.ppermute(theirs_half, "dp", swap)
    both = jnp.stack([mine_half, from_other])
    first = jnp.where(dp_at == 0, both[0], both[1])
    second = jnp.where(dp_at == 0, both[1], both[0])
    values = jnp.concatenate([first, second], axis=1) * scale
    delta = (values - goal.astype(jnp.float32)).astype(jnp.bfloat16)

    late_batch, _, _ = lax.optimization_barrier((token_batch, mine_half, other_normed))
    local_hidden = lax.all_to_all(late_batch, "fsdp", 1, 0, tiled=True)
    local_ratio = lax.all_gather(ratio, "fsdp", axis=0, tiled=True)
    local_delta = lax.all_gather(delta, "fsdp", axis=0, tiled=True)
    local_xhat = local_hidden.astype(jnp.float32) * local_ratio
    g_f = g_shard.astype(jnp.float32)
    local_normed = (local_xhat * g_f[None, :]).astype(jnp.bfloat16)
    sq_normed = jnp.square(local_normed.astype(jnp.float32)).astype(jnp.bfloat16)
    sq_delta = jnp.square(local_delta.astype(jnp.float32)).astype(jnp.bfloat16)
    fisher = jnp.einsum("td,th->dh", sq_normed, sq_delta, preferred_element_type=jnp.float32)
    back = jnp.einsum("th,dh->td", local_delta, w_shard, preferred_element_type=jnp.float32) * scale
    gain_info = jnp.sum(jnp.square(back * local_xhat), axis=0)

    n_pieces = n_t * n_dp
    piece = rows // n_pieces
    flat = piece * heads
    lane = 128
    tail_pad = -(2 * piece) % lane
    pack = jnp.concatenate(
        [
            (fisher * w_shard.astype(jnp.float32)).reshape(n_pieces, flat),
            fisher.reshape(n_pieces, flat),
            (gain_info * g_f).reshape(n_pieces, piece),
            gain_info.reshape(n_pieces, piece),
            jnp.zeros((n_pieces, tail_pad), jnp.float32),
        ],
        axis=1,
    )
    parts = lax.all_to_all(pack, ("dp", "template"), 0, 0, tiled=True)
    total = jnp.sum(parts, axis=0)
    quotient = total[:flat] / total[flat : 2 * flat]
    gain_quotient = total[2 * flat : 2 * flat + piece] / total[2 * flat + piece : 2 * flat + 2 * piece]
    done = jnp.concatenate([quotient, gain_quotient, jnp.zeros((-(flat + piece) % lane,), jnp.float32)])
    spread = lax.all_to_all(jnp.broadcast_to(done[None], (n_t,) + done.shape), "template", 0, 0, tiled=True)
    merged = spread[:, :flat].reshape(n_t * piece, heads)
    merged_gain = spread[:, flat : flat + piece].reshape(n_t * piece)
    return merged, merged_gain


def solution(mesh):
    in_specs = (
        P("template", ("fsdp", "dp"), None),
        P("template", ("fsdp", "dp"), None),
        P("template", "fsdp", None),
        P("template", "fsdp"),
    )
    out_specs = (P(("fsdp", "dp"), None), P(("fsdp", "dp")))
    return jax.shard_map(body, mesh=mesh, in_specs=in_specs, out_specs=out_specs, check_vma=False)
```

```python
import math

import jax
import jax.numpy as jnp
from jax import lax
from jax.sharding import PartitionSpec as P


def body(hidden, target, weight, gain):
    token_batch = hidden[0]
    goal = target[0]
    w_shard = weight[0]
    g_shard = gain[0]
    width = token_batch.shape[1]
    rows = w_shard.shape[0]
    heads = w_shard.shape[1]
    scale = 1.0 / math.sqrt(width)
    n_t = lax.axis_size("template")
    n_dp = lax.axis_size("dp")

    hidden_f = token_batch.astype(jnp.float32)
    ratio = lax.rsqrt(jnp.mean(jnp.square(hidden_f), axis=1, keepdims=True) + 1e-05)
    swap = [(i, (i + 1) % n_dp) for i in range(n_dp)]
    other_hidden = lax.ppermute(token_batch, "dp", swap)
    other_f = other_hidden.astype(jnp.float32)
    other_ratio = lax.rsqrt(jnp.mean(jnp.square(other_f), axis=1, keepdims=True) + 1e-05)
    half = heads // n_dp
    dp_at = lax.axis_index("dp")
    w_cols = lax.dynamic_slice_in_dim(w_shard, dp_at * half, half, 1)
    w_ext = jnp.concatenate([w_cols, g_shard.reshape(-1, half)], axis=0)
    gathered = lax.all_gather(w_ext, "fsdp", axis=0, tiled=False)
    w_half = gathered[:, :rows, :]
    g_full = gathered[:, rows:, :].reshape(-1).astype(jnp.float32)
    xhat = hidden_f * ratio
    normed = (xhat * g_full[None, :]).astype(jnp.bfloat16)
    other_normed = (other_f * other_ratio * g_full[None, :]).astype(jnp.bfloat16)
    n_blocks = gathered.shape[0]
    mine_half = jnp.einsum(
        "tfr,frh->th", normed.reshape(-1, n_blocks, rows), w_half, preferred_element_type=jnp.float32
    )
    theirs_half = jnp.einsum(
        "tfr,frh->th", other_normed.reshape(-1, n_blocks, rows), w_half, preferred_element_type=jnp.float32
    )
    from_other = lax.ppermute(theirs_half, "dp", swap)
    both = jnp.stack([mine_half, from_other])
    first = jnp.where(dp_at == 0, both[0], both[1])
    second = jnp.where(dp_at == 0, both[1], both[0])
    values = jnp.concatenate([first, second], axis=1) * scale
    delta = (values - goal.astype(jnp.float32)).astype(jnp.bfloat16)

    late_batch, _, _ = lax.optimization_barrier((token_batch, mine_half, other_normed))
    local_hidden = lax.all_to_all(late_batch, "fsdp", 1, 0, tiled=True)
    local_ratio = lax.all_gather(ratio, "fsdp", axis=0, tiled=True)
    local_delta = lax.all_gather(delta, "fsdp", axis=0, tiled=True)
    local_xhat = local_hidden.astype(jnp.float32) * local_ratio
    g_f = g_shard.astype(jnp.float32)
    local_normed = (local_xhat * g_f[None, :]).astype(jnp.bfloat16)
    sq_normed = jnp.square(local_normed.astype(jnp.float32)).astype(jnp.bfloat16)
    sq_delta = jnp.square(local_delta.astype(jnp.float32)).astype(jnp.bfloat16)
    fisher = jnp.einsum("td,th->dh", sq_normed, sq_delta, preferred_element_type=jnp.float32)
    back = jnp.einsum("th,dh->td", local_delta, w_shard, preferred_element_type=jnp.float32) * scale
    gain_info = jnp.sum(jnp.square(back * local_xhat), axis=0)

    extra = jnp.zeros((rows, 128), jnp.float32)
    extra = extra.at[:, 0].set(gain_info * g_f).at[:, 1].set(gain_info)
    pack = jnp.concatenate([fisher * w_shard.astype(jnp.float32), fisher, extra], axis=1)
    cols = pack.shape[1]
    piece = rows // (n_t * n_dp)
    pack = pack.reshape(n_t * n_dp, piece, cols)
    parts = lax.all_to_all(pack, ("dp", "template"), 0, 0, tiled=True)
    total = jnp.sum(parts, axis=0)
    ratio_block = jnp.zeros((piece, 128), jnp.float32).at[:, 0].set(total[:, 2 * heads] / total[:, 2 * heads + 1])
    done = jnp.concatenate([total[:, :heads] / total[:, heads : 2 * heads], ratio_block], axis=1)
    spread = lax.all_to_all(jnp.broadcast_to(done[None], (n_t,) + done.shape), "template", 0, 0, tiled=True)
    full = spread.reshape(n_t * piece, done.shape[1])
    merged = full[:, :heads]
    merged_gain = full[:, heads]
    return merged, merged_gain


def solution(mesh):
    in_specs = (
        P("template", ("fsdp", "dp"), None),
        P("template", ("fsdp", "dp"), None),
        P("template", "fsdp", None),
        P("template", "fsdp"),
    )
    out_specs = (P(("fsdp", "dp"), None), P(("fsdp", "dp")))
    return jax.shard_map(body, mesh=mesh, in_specs=in_specs, out_specs=out_specs, check_vma=False)
```

```python
import math

import jax
import jax.numpy as jnp
from jax import lax
from jax.sharding import PartitionSpec as P


def body(hidden, target, weight, gain):
    token_batch = hidden[0]
    goal = target[0]
    w_shard = weight[0]
    g_shard = gain[0]
    width = token_batch.shape[1]
    rows = w_shard.shape[0]
    heads = w_shard.shape[1]
    scale = 1.0 / math.sqrt(width)
    n_t = lax.axis_size("template")
    n_dp = lax.axis_size("dp")

    hidden_f = token_batch.astype(jnp.float32)
    ratio = lax.rsqrt(jnp.mean(jnp.square(hidden_f), axis=1, keepdims=True) + 1e-05)
    swap = [(i, (i + 1) % n_dp) for i in range(n_dp)]
    other_hidden = lax.ppermute(token_batch, "dp", swap)
    other_f = other_hidden.astype(jnp.float32)
    other_ratio = lax.rsqrt(jnp.mean(jnp.square(other_f), axis=1, keepdims=True) + 1e-05)
    half = heads // n_dp
    dp_at = lax.axis_index("dp")
    w_cols = lax.dynamic_slice_in_dim(w_shard, dp_at * half, half, 1)
    w_ext = jnp.concatenate([w_cols, g_shard.reshape(-1, half)], axis=0)
    gathered = lax.all_gather(w_ext, "fsdp", axis=0, tiled=False)
    w_half = gathered[:, :rows, :]
    g_full = gathered[:, rows:, :].reshape(-1).astype(jnp.float32)
    xhat = hidden_f * ratio
    normed = (xhat * g_full[None, :]).astype(jnp.bfloat16)
    other_normed = (other_f * other_ratio * g_full[None, :]).astype(jnp.bfloat16)
    n_blocks = gathered.shape[0]
    mine_half = jnp.einsum(
        "tfr,frh->th", normed.reshape(-1, n_blocks, rows), w_half, preferred_element_type=jnp.float32
    )
    theirs_half = jnp.einsum(
        "tfr,frh->th", other_normed.reshape(-1, n_blocks, rows), w_half, preferred_element_type=jnp.float32
    )
    from_other = lax.ppermute(theirs_half, "dp", swap)
    both = jnp.stack([mine_half, from_other])
    first = jnp.where(dp_at == 0, both[0], both[1])
    second = jnp.where(dp_at == 0, both[1], both[0])
    values = jnp.concatenate([first, second], axis=1) * scale
    delta = (values - goal.astype(jnp.float32)).astype(jnp.bfloat16)

    late_batch, _ = lax.optimization_barrier((token_batch, theirs_half))
    local_hidden = lax.all_to_all(late_batch, "fsdp", 1, 0, tiled=True)
    local_ratio = lax.all_gather(ratio, "fsdp", axis=0, tiled=True)
    local_delta = lax.all_gather(delta, "fsdp", axis=0, tiled=True)
    local_xhat = local_hidden.astype(jnp.float32) * local_ratio
    g_f = g_shard.astype(jnp.float32)
    local_normed = (local_xhat * g_f[None, :]).astype(jnp.bfloat16)
    sq_normed = jnp.square(local_normed.astype(jnp.float32)).astype(jnp.bfloat16)
    sq_delta = jnp.square(local_delta.astype(jnp.float32)).astype(jnp.bfloat16)
    fisher = jnp.einsum("td,th->dh", sq_normed, sq_delta, preferred_element_type=jnp.float32)
    back = jnp.einsum("th,dh->td", local_delta, w_shard, preferred_element_type=jnp.float32) * scale
    gain_info = jnp.sum(jnp.square(back * local_xhat), axis=0)

    extra = jnp.zeros((rows, 128), jnp.float32)
    extra = extra.at[:, 0].set(gain_info * g_f).at[:, 1].set(gain_info)
    pack = jnp.concatenate([fisher * w_shard.astype(jnp.float32), fisher, extra], axis=1)
    cols = pack.shape[1]
    piece = rows // (n_t * n_dp)
    pack = pack.reshape(n_t * n_dp, piece, cols)
    parts = lax.all_to_all(pack, ("dp", "template"), 0, 0, tiled=True)
    total = jnp.sum(parts, axis=0)
    ratio_block = jnp.zeros((piece, 128), jnp.float32).at[:, 0].set(total[:, 2 * heads] / total[:, 2 * heads + 1])
    done = jnp.concatenate([total[:, :heads] / total[:, heads : 2 * heads], ratio_block], axis=1)
    spread = lax.all_to_all(jnp.broadcast_to(done[None], (n_t,) + done.shape), "template", 0, 0, tiled=True)
    full = spread.reshape(n_t * piece, done.shape[1])
    merged = full[:, :heads]
    merged_gain = full[:, heads]
    return merged, merged_gain


def solution(mesh):
    in_specs = (
        P("template", ("fsdp", "dp"), None),
        P("template", ("fsdp", "dp"), None),
        P("template", "fsdp", None),
        P("template", "fsdp"),
    )
    out_specs = (P(("fsdp", "dp"), None), P(("fsdp", "dp")))
    return jax.shard_map(body, mesh=mesh, in_specs=in_specs, out_specs=out_specs, check_vma=False)
```

```python
import math

import jax
import jax.numpy as jnp
from jax import lax
from jax.sharding import PartitionSpec as P


def body(hidden, target, weight, gain):
    token_batch = hidden[0]
    goal = target[0]
    w_shard = weight[0]
    g_shard = gain[0]
    width = token_batch.shape[1]
    rows = w_shard.shape[0]
    heads = w_shard.shape[1]
    scale = 1.0 / math.sqrt(width)
    n_t = lax.axis_size("template")
    n_dp = lax.axis_size("dp")

    hidden_f = token_batch.astype(jnp.float32)
    ratio = lax.rsqrt(jnp.mean(jnp.square(hidden_f), axis=1, keepdims=True) + 1e-05)
    swap = [(i, (i + 1) % n_dp) for i in range(n_dp)]
    other_hidden = lax.ppermute(token_batch, "dp", swap)
    other_f = other_hidden.astype(jnp.float32)
    other_ratio = lax.rsqrt(jnp.mean(jnp.square(other_f), axis=1, keepdims=True) + 1e-05)
    half = heads // n_dp
    dp_at = lax.axis_index("dp")
    w_cols = lax.dynamic_slice_in_dim(w_shard, dp_at * half, half, 1)
    w_ext = jnp.concatenate([w_cols, g_shard.reshape(-1, half)], axis=0)
    gathered = lax.all_gather(w_ext, "fsdp", axis=0, tiled=False)
    w_half = gathered[:, :rows, :]
    g_full = gathered[:, rows:, :].reshape(-1).astype(jnp.float32)
    xhat = hidden_f * ratio
    normed = (xhat * g_full[None, :]).astype(jnp.bfloat16)
    other_normed = (other_f * other_ratio * g_full[None, :]).astype(jnp.bfloat16)
    n_blocks = gathered.shape[0]
    mine_half = jnp.einsum(
        "tfr,frh->th", normed.reshape(-1, n_blocks, rows), w_half, preferred_element_type=jnp.float32
    )
    theirs_half = jnp.einsum(
        "tfr,frh->th", other_normed.reshape(-1, n_blocks, rows), w_half, preferred_element_type=jnp.float32
    )
    from_other = lax.ppermute(theirs_half, "dp", swap)
    both = jnp.stack([mine_half, from_other])
    first = jnp.where(dp_at == 0, both[0], both[1])
    second = jnp.where(dp_at == 0, both[1], both[0])
    values = jnp.concatenate([first, second], axis=1) * scale
    delta = (values - goal.astype(jnp.float32)).astype(jnp.bfloat16)

    n_f = lax.axis_size("fsdp")
    by_dest = jnp.transpose(token_batch.reshape(token_batch.shape[0], n_f, rows), (1, 0, 2))
    late_batch, _ = lax.optimization_barrier((by_dest, theirs_half))
    local_hidden = lax.all_to_all(late_batch, "fsdp", 0, 0, tiled=True).reshape(-1, rows)
    local_ratio = lax.all_gather(ratio, "fsdp", axis=0, tiled=True)
    local_delta = lax.all_gather(delta, "fsdp", axis=0, tiled=True)
    local_xhat = local_hidden.astype(jnp.float32) * local_ratio
    g_f = g_shard.astype(jnp.float32)
    local_normed = (local_xhat * g_f[None, :]).astype(jnp.bfloat16)
    sq_normed = jnp.square(local_normed.astype(jnp.float32)).astype(jnp.bfloat16)
    sq_delta = jnp.square(local_delta.astype(jnp.float32)).astype(jnp.bfloat16)
    fisher = jnp.einsum("td,th->dh", sq_normed, sq_delta, preferred_element_type=jnp.float32)
    back = jnp.einsum("th,dh->td", local_delta, w_shard, preferred_element_type=jnp.float32) * scale
    gain_info = jnp.sum(jnp.square(back * local_xhat), axis=0)

    extra = jnp.zeros((rows, 128), jnp.float32)
    extra = extra.at[:, 0].set(gain_info * g_f).at[:, 1].set(gain_info)
    pack = jnp.concatenate([fisher * w_shard.astype(jnp.float32), fisher, extra], axis=1)
    cols = pack.shape[1]
    piece = rows // (n_t * n_dp)
    pack = pack.reshape(n_t * n_dp, piece, cols)
    parts = lax.all_to_all(pack, ("dp", "template"), 0, 0, tiled=True)
    total = jnp.sum(parts, axis=0)
    ratio_block = jnp.zeros((piece, 128), jnp.float32).at[:, 0].set(total[:, 2 * heads] / total[:, 2 * heads + 1])
    done = jnp.concatenate([total[:, :heads] / total[:, heads : 2 * heads], ratio_block], axis=1)
    spread = lax.all_to_all(jnp.broadcast_to(done[None], (n_t,) + done.shape), "template", 0, 0, tiled=True)
    full = spread.reshape(n_t * piece, done.shape[1])
    merged = full[:, :heads]
    merged_gain = full[:, heads]
    return merged, merged_gain


def solution(mesh):
    in_specs = (
        P("template", ("fsdp", "dp"), None),
        P("template", ("fsdp", "dp"), None),
        P("template", "fsdp", None),
        P("template", "fsdp"),
    )
    out_specs = (P(("fsdp", "dp"), None), P(("fsdp", "dp")))
    return jax.shard_map(body, mesh=mesh, in_specs=in_specs, out_specs=out_specs, check_vma=False)
```

```python
import math

import jax
import jax.numpy as jnp
from jax import lax
from jax.sharding import PartitionSpec as P


def body(hidden, target, weight, gain):
    token_batch = hidden[0]
    goal = target[0]
    w_shard = weight[0]
    g_shard = gain[0]
    width = token_batch.shape[1]
    rows = w_shard.shape[0]
    heads = w_shard.shape[1]
    scale = 1.0 / math.sqrt(width)
    n_t = lax.axis_size("template")
    n_dp = lax.axis_size("dp")

    hidden_f = token_batch.astype(jnp.float32)
    ratio = lax.rsqrt(jnp.mean(jnp.square(hidden_f), axis=1, keepdims=True) + 1e-05)
    swap = [(i, (i + 1) % n_dp) for i in range(n_dp)]
    other_hidden = lax.ppermute(token_batch, "dp", swap)
    other_f = other_hidden.astype(jnp.float32)
    other_ratio = lax.rsqrt(jnp.mean(jnp.square(other_f), axis=1, keepdims=True) + 1e-05)
    half = heads // n_dp
    dp_at = lax.axis_index("dp")
    w_cols = jnp.where(dp_at == 0, w_shard[:, :half], w_shard[:, half:])
    w_ext = jnp.concatenate([w_cols, g_shard.reshape(-1, half)], axis=0)
    gathered = lax.all_gather(w_ext, "fsdp", axis=0, tiled=False)
    w_half = gathered[:, :rows, :]
    g_full = gathered[:, rows:, :].reshape(-1).astype(jnp.float32)
    xhat = hidden_f * ratio
    normed = (xhat * g_full[None, :]).astype(jnp.bfloat16)
    other_normed = (other_f * other_ratio * g_full[None, :]).astype(jnp.bfloat16)
    n_blocks = gathered.shape[0]
    mine_half = jnp.einsum(
        "tfr,frh->th", normed.reshape(-1, n_blocks, rows), w_half, preferred_element_type=jnp.float32
    )
    theirs_half = jnp.einsum(
        "tfr,frh->th", other_normed.reshape(-1, n_blocks, rows), w_half, preferred_element_type=jnp.float32
    )
    from_other = lax.ppermute(theirs_half, "dp", swap)
    both = jnp.stack([mine_half, from_other])
    first = jnp.where(dp_at == 0, both[0], both[1])
    second = jnp.where(dp_at == 0, both[1], both[0])
    values = jnp.concatenate([first, second], axis=1) * scale
    delta = (values - goal.astype(jnp.float32)).astype(jnp.bfloat16)

    n_f = lax.axis_size("fsdp")
    by_dest = jnp.transpose(token_batch.reshape(token_batch.shape[0], n_f, rows), (1, 0, 2))
    late_batch, _ = lax.optimization_barrier((by_dest, theirs_half))
    local_hidden = lax.all_to_all(late_batch, "fsdp", 0, 0, tiled=True).reshape(-1, rows)
    local_ratio = lax.all_gather(ratio, "fsdp", axis=0, tiled=True)
    local_delta = lax.all_gather(delta, "fsdp", axis=0, tiled=True)
    local_xhat = local_hidden.astype(jnp.float32) * local_ratio
    g_f = g_shard.astype(jnp.float32)
    local_normed = (local_xhat * g_f[None, :]).astype(jnp.bfloat16)
    sq_normed = jnp.square(local_normed.astype(jnp.float32)).astype(jnp.bfloat16)
    sq_delta = jnp.square(local_delta.astype(jnp.float32)).astype(jnp.bfloat16)
    fisher = jnp.einsum("td,th->dh", sq_normed, sq_delta, preferred_element_type=jnp.float32)
    back = jnp.einsum("th,dh->td", local_delta, w_shard, preferred_element_type=jnp.float32) * scale
    gain_info = jnp.sum(jnp.square(back * local_xhat), axis=0)

    extra = jnp.concatenate(
        [(gain_info * g_f)[:, None], gain_info[:, None], jnp.zeros((rows, 126), jnp.float32)], axis=1
    )
    pack = jnp.concatenate([fisher * w_shard.astype(jnp.float32), fisher, extra], axis=1)
    cols = pack.shape[1]
    piece = rows // (n_t * n_dp)
    pack = pack.reshape(n_t * n_dp, piece, cols)
    parts = lax.all_to_all(pack, ("dp", "template"), 0, 0, tiled=True)
    total = jnp.sum(parts, axis=0)
    ratio_block = jnp.zeros((piece, 128), jnp.float32).at[:, 0].set(total[:, 2 * heads] / total[:, 2 * heads + 1])
    done = jnp.concatenate([total[:, :heads] / total[:, heads : 2 * heads], ratio_block], axis=1)
    spread = lax.all_to_all(jnp.broadcast_to(done[None], (n_t,) + done.shape), "template", 0, 0, tiled=True)
    full = spread.reshape(n_t * piece, done.shape[1])
    merged = full[:, :heads]
    merged_gain = full[:, heads]
    return merged, merged_gain


def solution(mesh):
    in_specs = (
        P("template", ("fsdp", "dp"), None),
        P("template", ("fsdp", "dp"), None),
        P("template", "fsdp", None),
        P("template", "fsdp"),
    )
    out_specs = (P(("fsdp", "dp"), None), P(("fsdp", "dp")))
    return jax.shard_map(body, mesh=mesh, in_specs=in_specs, out_specs=out_specs, check_vma=False)
```

```python
import math

import jax
import jax.numpy as jnp
from jax import lax
from jax.sharding import PartitionSpec as P


def body(hidden, target, weight, gain):
    token_batch = hidden[0]
    goal = target[0]
    w_shard = weight[0]
    g_shard = gain[0]
    width = token_batch.shape[1]
    rows = w_shard.shape[0]
    heads = w_shard.shape[1]
    scale = 1.0 / math.sqrt(width)
    n_t = lax.axis_size("template")
    n_dp = lax.axis_size("dp")

    hidden_f = token_batch.astype(jnp.float32)
    ratio = lax.rsqrt(jnp.mean(jnp.square(hidden_f), axis=1, keepdims=True) + 1e-05)
    swap = [(i, (i + 1) % n_dp) for i in range(n_dp)]
    other_hidden = lax.ppermute(token_batch, "dp", swap)
    other_f = other_hidden.astype(jnp.float32)
    other_ratio = lax.rsqrt(jnp.mean(jnp.square(other_f), axis=1, keepdims=True) + 1e-05)
    half = heads // n_dp
    dp_at = lax.axis_index("dp")
    w_cols = lax.dynamic_slice_in_dim(w_shard, dp_at * half, half, 1)
    w_ext = jnp.concatenate([w_cols, g_shard.reshape(-1, half)], axis=0)
    gathered = lax.all_gather(w_ext, "fsdp", axis=0, tiled=False)
    w_half = gathered[:, :rows, :]
    g_full = gathered[:, rows:, :].reshape(-1).astype(jnp.float32)
    xhat = hidden_f * ratio
    normed = (xhat * g_full[None, :]).astype(jnp.bfloat16)
    other_normed = (other_f * other_ratio * g_full[None, :]).astype(jnp.bfloat16)
    n_blocks = gathered.shape[0]
    mine_half = jnp.einsum(
        "tfr,frh->th", normed.reshape(-1, n_blocks, rows), w_half, preferred_element_type=jnp.float32
    )
    theirs_half = jnp.einsum(
        "tfr,frh->th", other_normed.reshape(-1, n_blocks, rows), w_half, preferred_element_type=jnp.float32
    )
    from_other = lax.ppermute(theirs_half, "dp", swap)
    both = jnp.stack([mine_half, from_other])
    first = jnp.where(dp_at == 0, both[0], both[1])
    second = jnp.where(dp_at == 0, both[1], both[0])
    values = jnp.concatenate([first, second], axis=1) * scale
    delta = (values - goal.astype(jnp.float32)).astype(jnp.bfloat16)

    n_f = lax.axis_size("fsdp")
    by_dest = jnp.transpose(token_batch.reshape(token_batch.shape[0], n_f, rows), (1, 0, 2))
    late_batch, _ = lax.optimization_barrier((by_dest, theirs_half))
    local_hidden = lax.all_to_all(late_batch, "fsdp", 0, 0, tiled=True).reshape(-1, rows)
    r_hi = ratio[:, 0].astype(jnp.bfloat16)
    r_rest = ratio[:, 0] - r_hi.astype(jnp.float32)
    r_mid = r_rest.astype(jnp.bfloat16)
    r_lo = (r_rest - r_mid.astype(jnp.float32)).astype(jnp.bfloat16)
    n_tok = delta.shape[0]
    side = jnp.concatenate([r_hi, r_mid, r_lo, jnp.zeros((heads - 3 * n_tok,), jnp.bfloat16)])
    side = jnp.concatenate([side[None, :], jnp.zeros((15, heads), jnp.bfloat16)], axis=0)
    carried = lax.all_gather(jnp.concatenate([delta, side], axis=0), "fsdp", axis=0, tiled=False)
    local_delta = carried[:, :n_tok, :].reshape(-1, heads)
    parts = carried[:, n_tok, : 3 * n_tok].astype(jnp.float32).reshape(-1, 3, n_tok)
    local_ratio = ((parts[:, 0] + parts[:, 1]) + parts[:, 2]).reshape(-1, 1)
    local_xhat = local_hidden.astype(jnp.float32) * local_ratio
    g_f = g_shard.astype(jnp.float32)
    local_normed = (local_xhat * g_f[None, :]).astype(jnp.bfloat16)
    sq_normed = jnp.square(local_normed.astype(jnp.float32)).astype(jnp.bfloat16)
    sq_delta = jnp.square(local_delta.astype(jnp.float32)).astype(jnp.bfloat16)
    fisher = jnp.einsum("td,th->dh", sq_normed, sq_delta, preferred_element_type=jnp.float32)
    back = jnp.einsum("th,dh->td", local_delta, w_shard, preferred_element_type=jnp.float32) * scale
    gain_info = jnp.sum(jnp.square(back * local_xhat), axis=0)

    extra = jnp.zeros((rows, 128), jnp.float32)
    extra = extra.at[:, 0].set(gain_info * g_f).at[:, 1].set(gain_info)
    pack = jnp.concatenate([fisher * w_shard.astype(jnp.float32), fisher, extra], axis=1)
    cols = pack.shape[1]
    piece = rows // (n_t * n_dp)
    pack = pack.reshape(n_t * n_dp, piece, cols)
    parts = lax.all_to_all(pack, ("dp", "template"), 0, 0, tiled=True)
    total = jnp.sum(parts, axis=0)
    ratio_block = jnp.zeros((piece, 128), jnp.float32).at[:, 0].set(total[:, 2 * heads] / total[:, 2 * heads + 1])
    done = jnp.concatenate([total[:, :heads] / total[:, heads : 2 * heads], ratio_block], axis=1)
    spread = lax.all_to_all(jnp.broadcast_to(done[None], (n_t,) + done.shape), "template", 0, 0, tiled=True)
    full = spread.reshape(n_t * piece, done.shape[1])
    merged = full[:, :heads]
    merged_gain = full[:, heads]
    return merged, merged_gain


def solution(mesh):
    in_specs = (
        P("template", ("fsdp", "dp"), None),
        P("template", ("fsdp", "dp"), None),
        P("template", "fsdp", None),
        P("template", "fsdp"),
    )
    out_specs = (P(("fsdp", "dp"), None), P(("fsdp", "dp")))
    return jax.shard_map(body, mesh=mesh, in_specs=in_specs, out_specs=out_specs, check_vma=False)
```

```python
import math

import jax
import jax.numpy as jnp
from jax import lax
from jax.sharding import PartitionSpec as P


def body(hidden, target, weight, gain):
    token_batch = hidden[0]
    goal = target[0]
    w_shard = weight[0]
    g_shard = gain[0]
    width = token_batch.shape[1]
    rows = w_shard.shape[0]
    heads = w_shard.shape[1]
    scale = 1.0 / math.sqrt(width)
    n_t = lax.axis_size("template")
    n_dp = lax.axis_size("dp")

    hidden_f = token_batch.astype(jnp.float32)
    ratio = lax.rsqrt(jnp.mean(jnp.square(hidden_f), axis=1, keepdims=True) + 1e-05)
    swap = [(i, (i + 1) % n_dp) for i in range(n_dp)]
    other_hidden = lax.ppermute(token_batch, "dp", swap)
    other_f = other_hidden.astype(jnp.float32)
    other_ratio = lax.rsqrt(jnp.mean(jnp.square(other_f), axis=1, keepdims=True) + 1e-05)
    half = heads // n_dp
    dp_at = lax.axis_index("dp")
    w_cols = lax.dynamic_slice_in_dim(w_shard, dp_at * half, half, 1)
    w_ext = jnp.concatenate([w_cols, g_shard.reshape(-1, half)], axis=0)
    gathered = lax.all_gather(w_ext, "fsdp", axis=0, tiled=False)
    w_half = gathered[:, :rows, :]
    g_full = gathered[:, rows:, :].reshape(-1).astype(jnp.float32)
    xhat = hidden_f * ratio
    normed = (xhat * g_full[None, :]).astype(jnp.bfloat16)
    other_normed = (other_f * other_ratio * g_full[None, :]).astype(jnp.bfloat16)
    n_blocks = gathered.shape[0]
    mine_half = jnp.einsum(
        "tfr,frh->th", normed.reshape(-1, n_blocks, rows), w_half, preferred_element_type=jnp.float32
    )
    theirs_half = jnp.einsum(
        "tfr,frh->th", other_normed.reshape(-1, n_blocks, rows), w_half, preferred_element_type=jnp.float32
    )
    from_other = lax.ppermute(theirs_half, "dp", swap)
    both = jnp.stack([mine_half, from_other])
    first = jnp.where(dp_at == 0, both[0], both[1])
    second = jnp.where(dp_at == 0, both[1], both[0])
    values = jnp.concatenate([first, second], axis=1) * scale
    delta = (values - goal.astype(jnp.float32)).astype(jnp.bfloat16)

    n_f = lax.axis_size("fsdp")
    by_dest = jnp.transpose(token_batch.reshape(token_batch.shape[0], n_f, rows), (1, 0, 2))
    late_batch, _ = lax.optimization_barrier((by_dest, theirs_half))
    local_hidden = lax.all_to_all(late_batch, "fsdp", 0, 0, tiled=True).reshape(-1, rows)
    local_ratio = lax.all_gather(ratio, "fsdp", axis=0, tiled=True)
    local_delta = lax.all_gather(delta, "fsdp", axis=0, tiled=True)
    local_xhat = local_hidden.astype(jnp.float32) * local_ratio
    g_f = g_shard.astype(jnp.float32)
    local_normed = (local_xhat * g_f[None, :]).astype(jnp.bfloat16)
    sq_normed = jnp.square(local_normed.astype(jnp.float32)).astype(jnp.bfloat16)
    sq_delta = jnp.square(local_delta.astype(jnp.float32)).astype(jnp.bfloat16)
    fisher = jnp.einsum("td,th->dh", sq_normed, sq_delta, preferred_element_type=jnp.float32)
    back = jnp.einsum("th,dh->td", local_delta, w_shard, preferred_element_type=jnp.float32) * scale
    gain_info = jnp.sum(jnp.square(back * local_xhat), axis=0)

    n_pieces = n_t * n_dp
    piece = rows // n_pieces
    flat = piece * heads
    pack = jnp.concatenate(
        [
            (fisher * w_shard.astype(jnp.float32)).reshape(n_pieces, flat),
            fisher.reshape(n_pieces, flat),
            (gain_info * g_f).reshape(n_pieces, piece),
            gain_info.reshape(n_pieces, piece),
            jnp.zeros((n_pieces, -(2 * piece) % 128), jnp.float32),
        ],
        axis=1,
    )
    parts = lax.all_to_all(pack, ("dp", "template"), 0, 0, tiled=True)
    sums = jnp.sum(parts, axis=0)
    total = jnp.concatenate(
        [sums[:flat].reshape(piece, heads), sums[flat : 2 * flat].reshape(piece, heads),
         sums[2 * flat : 2 * flat + 2 * piece].reshape(2, piece).T], axis=1
    )
    ratio_block = jnp.zeros((piece, 128), jnp.float32).at[:, 0].set(total[:, 2 * heads] / total[:, 2 * heads + 1])
    done = jnp.concatenate([total[:, :heads] / total[:, heads : 2 * heads], ratio_block], axis=1)
    spread = lax.all_to_all(jnp.broadcast_to(done[None], (n_t,) + done.shape), "template", 0, 0, tiled=True)
    full = spread.reshape(n_t * piece, done.shape[1])
    merged = full[:, :heads]
    merged_gain = full[:, heads]
    return merged, merged_gain


def solution(mesh):
    in_specs = (
        P("template", ("fsdp", "dp"), None),
        P("template", ("fsdp", "dp"), None),
        P("template", "fsdp", None),
        P("template", "fsdp"),
    )
    out_specs = (P(("fsdp", "dp"), None), P(("fsdp", "dp")))
    return jax.shard_map(body, mesh=mesh, in_specs=in_specs, out_specs=out_specs, check_vma=False)
```

```python
import math

import jax
import jax.numpy as jnp
from jax import lax
from jax.sharding import PartitionSpec as P


def body(hidden, target, weight, gain):
    token_batch = hidden[0]
    goal = target[0]
    w_shard = weight[0]
    g_shard = gain[0]
    width = token_batch.shape[1]
    rows = w_shard.shape[0]
    heads = w_shard.shape[1]
    scale = 1.0 / math.sqrt(width)
    n_t = lax.axis_size("template")
    n_dp = lax.axis_size("dp")

    hidden_f = token_batch.astype(jnp.float32)
    ratio = lax.rsqrt(jnp.mean(jnp.square(hidden_f), axis=1, keepdims=True) + 1e-05)
    swap = [(i, (i + 1) % n_dp) for i in range(n_dp)]
    other_hidden = lax.ppermute(token_batch, "dp", swap)
    other_f = other_hidden.astype(jnp.float32)
    other_ratio = lax.rsqrt(jnp.mean(jnp.square(other_f), axis=1, keepdims=True) + 1e-05)
    half = heads // n_dp
    dp_at = lax.axis_index("dp")
    w_cols = lax.dynamic_slice_in_dim(w_shard, dp_at * half, half, 1)
    w_ext = jnp.concatenate([w_cols, g_shard.reshape(-1, half)], axis=0)
    gathered = lax.all_gather(w_ext, "fsdp", axis=0, tiled=False)
    w_half = gathered[:, :rows, :]
    g_full = gathered[:, rows:, :].reshape(-1).astype(jnp.float32)
    xhat = hidden_f * ratio
    normed = (xhat * g_full[None, :]).astype(jnp.bfloat16)
    other_normed = (other_f * other_ratio * g_full[None, :]).astype(jnp.bfloat16)
    n_blocks = gathered.shape[0]
    mine_half = jnp.einsum(
        "tfr,frh->th", normed.reshape(-1, n_blocks, rows), w_half, preferred_element_type=jnp.float32
    )
    theirs_half = jnp.einsum(
        "tfr,frh->th", other_normed.reshape(-1, n_blocks, rows), w_half, preferred_element_type=jnp.float32
    )
    from_other = lax.ppermute(theirs_half, "dp", swap)
    both = jnp.stack([mine_half, from_other])
    first = jnp.where(dp_at == 0, both[0], both[1])
    second = jnp.where(dp_at == 0, both[1], both[0])
    values = jnp.concatenate([first, second], axis=1) * scale
    delta = (values - goal.astype(jnp.float32)).astype(jnp.bfloat16)

    n_f = lax.axis_size("fsdp")
    by_dest = jnp.transpose(token_batch.reshape(token_batch.shape[0], n_f, rows), (1, 0, 2))
    late_batch, _ = lax.optimization_barrier((by_dest, other_normed))
    local_hidden = lax.all_to_all(late_batch, "fsdp", 0, 0, tiled=True).reshape(-1, rows)
    local_ratio = lax.all_gather(ratio, "fsdp", axis=0, tiled=True)
    local_delta = lax.all_gather(delta, "fsdp", axis=0, tiled=True)
    local_xhat = local_hidden.astype(jnp.float32) * local_ratio
    g_f = g_shard.astype(jnp.float32)
    local_normed = (local_xhat * g_f[None, :]).astype(jnp.bfloat16)
    sq_normed = jnp.square(local_normed.astype(jnp.float32)).astype(jnp.bfloat16)
    sq_delta = jnp.square(local_delta.astype(jnp.float32)).astype(jnp.bfloat16)
    fisher = jnp.einsum("td,th->dh", sq_normed, sq_delta, preferred_element_type=jnp.float32)
    back = jnp.einsum("th,dh->td", local_delta, w_shard, preferred_element_type=jnp.float32) * scale
    gain_info = jnp.sum(jnp.square(back * local_xhat), axis=0)

    extra = jnp.zeros((rows, 128), jnp.float32)
    extra = extra.at[:, 0].set(gain_info * g_f).at[:, 1].set(gain_info)
    pack = jnp.concatenate([fisher * w_shard.astype(jnp.float32), fisher, extra], axis=1)
    cols = pack.shape[1]
    piece = rows // (n_t * n_dp)
    pack = pack.reshape(n_t * n_dp, piece, cols)
    parts = lax.all_to_all(pack, ("dp", "template"), 0, 0, tiled=True)
    total = jnp.sum(parts, axis=0)
    ratio_block = jnp.zeros((piece, 128), jnp.float32).at[:, 0].set(total[:, 2 * heads] / total[:, 2 * heads + 1])
    done = jnp.concatenate([total[:, :heads] / total[:, heads : 2 * heads], ratio_block], axis=1)
    spread = lax.all_to_all(jnp.broadcast_to(done[None], (n_t,) + done.shape), "template", 0, 0, tiled=True)
    full = spread.reshape(n_t * piece, done.shape[1])
    merged = full[:, :heads]
    merged_gain = full[:, heads]
    return merged, merged_gain


def solution(mesh):
    in_specs = (
        P("template", ("fsdp", "dp"), None),
        P("template", ("fsdp", "dp"), None),
        P("template", "fsdp", None),
        P("template", "fsdp"),
    )
    out_specs = (P(("fsdp", "dp"), None), P(("fsdp", "dp")))
    return jax.shard_map(body, mesh=mesh, in_specs=in_specs, out_specs=out_specs, check_vma=False)
```

```python
import math

import jax
import jax.numpy as jnp
from jax import lax
from jax.sharding import PartitionSpec as P


def body(hidden, target, weight, gain):
    token_batch = hidden[0]
    goal = target[0]
    w_shard = weight[0]
    g_shard = gain[0]
    width = token_batch.shape[1]
    rows = w_shard.shape[0]
    heads = w_shard.shape[1]
    scale = 1.0 / math.sqrt(width)
    n_t = lax.axis_size("template")
    n_dp = lax.axis_size("dp")

    hidden_f = token_batch.astype(jnp.float32)
    ratio = lax.rsqrt(jnp.mean(jnp.square(hidden_f), axis=1, keepdims=True) + 1e-05)
    swap = [(i, (i + 1) % n_dp) for i in range(n_dp)]
    other_hidden = lax.ppermute(token_batch, "dp", swap)
    other_f = other_hidden.astype(jnp.float32)
    other_ratio = lax.rsqrt(jnp.mean(jnp.square(other_f), axis=1, keepdims=True) + 1e-05)
    half = heads // n_dp
    dp_at = lax.axis_index("dp")
    w_cols = lax.dynamic_slice_in_dim(w_shard, dp_at * half, half, 1)
    w_ext = jnp.concatenate([w_cols, g_shard.reshape(-1, half)], axis=0)
    gathered = lax.all_gather(w_ext, "fsdp", axis=0, tiled=False)
    w_half = gathered[:, :rows, :].reshape(-1, half)
    g_full = gathered[:, rows:, :].reshape(-1).astype(jnp.float32)
    xhat = hidden_f * ratio
    normed = (xhat * g_full[None, :]).astype(jnp.bfloat16)
    other_normed = (other_f * other_ratio * g_full[None, :]).astype(jnp.bfloat16)
    mine_half = jnp.dot(normed, w_half, preferred_element_type=jnp.float32)
    theirs_half = jnp.dot(other_normed, w_half, preferred_element_type=jnp.float32)
    from_other = lax.ppermute(theirs_half, "dp", swap)
    both = jnp.stack([mine_half, from_other])
    first = jnp.where(dp_at == 0, both[0], both[1])
    second = jnp.where(dp_at == 0, both[1], both[0])
    values = jnp.concatenate([first, second], axis=1) * scale
    delta = (values - goal.astype(jnp.float32)).astype(jnp.bfloat16)

    n_f = lax.axis_size("fsdp")
    by_dest = jnp.transpose(token_batch.reshape(token_batch.shape[0], n_f, rows), (1, 0, 2))
    late_batch, _ = lax.optimization_barrier((by_dest, theirs_half))
    local_hidden = lax.all_to_all(late_batch, "fsdp", 0, 0, tiled=True).reshape(-1, rows)
    local_ratio = lax.all_gather(ratio, "fsdp", axis=0, tiled=True)
    local_delta = lax.all_gather(delta, "fsdp", axis=0, tiled=True)
    local_xhat = local_hidden.astype(jnp.float32) * local_ratio
    g_f = g_shard.astype(jnp.float32)
    local_normed = (local_xhat * g_f[None, :]).astype(jnp.bfloat16)
    sq_normed = jnp.square(local_normed.astype(jnp.float32)).astype(jnp.bfloat16)
    sq_delta = jnp.square(local_delta.astype(jnp.float32)).astype(jnp.bfloat16)
    fisher = jnp.einsum("td,th->dh", sq_normed, sq_delta, preferred_element_type=jnp.float32)
    back = jnp.einsum("th,dh->td", local_delta, w_shard, preferred_element_type=jnp.float32) * scale
    gain_info = jnp.sum(jnp.square(back * local_xhat), axis=0)

    extra = jnp.zeros((rows, 128), jnp.float32)
    extra = extra.at[:, 0].set(gain_info * g_f).at[:, 1].set(gain_info)
    pack = jnp.concatenate([fisher * w_shard.astype(jnp.float32), fisher, extra], axis=1)
    cols = pack.shape[1]
    piece = rows // (n_t * n_dp)
    pack = pack.reshape(n_t * n_dp, piece, cols)
    parts = lax.all_to_all(pack, ("dp", "template"), 0, 0, tiled=True)
    total = jnp.sum(parts, axis=0)
    ratio_block = jnp.zeros((piece, 128), jnp.float32).at[:, 0].set(total[:, 2 * heads] / total[:, 2 * heads + 1])
    done = jnp.concatenate([total[:, :heads] / total[:, heads : 2 * heads], ratio_block], axis=1)
    spread = lax.all_to_all(jnp.broadcast_to(done[None], (n_t,) + done.shape), "template", 0, 0, tiled=True)
    full = spread.reshape(n_t * piece, done.shape[1])
    merged = full[:, :heads]
    merged_gain = full[:, heads]
    return merged, merged_gain


def solution(mesh):
    in_specs = (
        P("template", ("fsdp", "dp"), None),
        P("template", ("fsdp", "dp"), None),
        P("template", "fsdp", None),
        P("template", "fsdp"),
    )
    out_specs = (P(("fsdp", "dp"), None), P(("fsdp", "dp")))
    return jax.shard_map(body, mesh=mesh, in_specs=in_specs, out_specs=out_specs, check_vma=False)
```
